256 devices in a mesh: span: 8 (over y, x_hi), tm: 32 (over x_lo, z, core).
Axes of the slice: x: 4 (x_hi: 2, x_lo: 2; x = x_hi * 2 + x_lo), y: 4, z: 8, core: 2. Of those that a mesh axis runs over, the one named last changes fastest.
Arguments:
- launched: float32 [8, 2, 110, 8192], P(None, None, None, 'tm'), may hold values from -1.5 to 1.5
- coupling: float32 [8, 2, 2, 2, 110, 110], P('span'), may hold values from -2 to 2
- impulse: float32 [8, 2, 2, 2, 129], P('span'), may hold values from -1.5 to 1.5
- amplifier: float32 [8, 2, 110], P('span'), may hold values from 0.9 to 1.11
- nonlinear: float32 [8, 2, 2], P('span'), may hold values from 0.002 to 0.008
Outputs:
- monitored: float32 [8, 8, 2, 110, 8192], P('span', None, None, None, 'tm')
The draws below stay inside these ranges and needn't reach their ends.
All inputs are finite; a program needn't handle non-finite values.
Results may differ from the reference program's by a relative error of at most 0.0004.
Values sent between devices are 32-bit elements; how exact they have to be, the bound alone decides.
No kernel may reach another device: no remote copies, remote signals or barrier semaphores. Data moves between devices by JAX's collectives and lax.ppermute only.
A program may use at most 64 MiB of HBM per device.

```python
import math
import jax
import jax.numpy as jnp
from jax import lax

CH = 110
HALF = 64
STEPS = 2
SPANS = 2
SAMP = 256
FRAMES = 8
GROUPS = 8
N_SPAN = 8
N_TM = 32


def noise_field(key, shape, deviation):
    return deviation * jnp.clip(jax.random.normal(key, shape, jnp.float32), -3.0, 3.0)


def draw_launched(key, part):
    shape = (FRAMES, 2, CH, SAMP * N_TM)
    return noise_field(key, shape, 0.5)


def draw_coupling(key, part):
    shape = (N_SPAN, SPANS, STEPS, 2, CH, CH)
    deviation = 0.5 / (2.0 * CH) ** 0.5
    noise = noise_field(key, shape, deviation)
    identity = jnp.eye(CH, dtype=jnp.float32)
    component = (jnp.arange(2) == 0).astype(jnp.float32)
    return noise + 0.85 * component[:, None, None] * identity[None, :, :]


def draw_impulse(key, part):
    taps = 2 * HALF + 1
    shape = (N_SPAN, SPANS, STEPS, 2, taps)
    deviation = 0.6 / (2.0 * taps) ** 0.5
    noise = noise_field(key, shape, deviation)
    centre = (jnp.arange(taps) == HALF).astype(jnp.float32)
    component = (jnp.arange(2) == 0).astype(jnp.float32)
    return noise + 0.8 * component[:, None] * centre[None, :]


def draw_amplifier(key, part):
    shape = (N_SPAN, SPANS, CH)
    exponent = jnp.clip(0.05 * jax.random.normal(key, shape, jnp.float32), -0.1, 0.1)
    return jnp.exp(exponent)


def block_scale(stream_key, extent, split, least, high):
    gain = 1.0
    for dim, shards_of in split:
        steps = jax.random.uniform(jax.random.fold_in(jax.random.fold_in(stream_key, 6), dim), (shards_of,), jnp.float32, least / len(split), high / len(split))
        gain = gain * jnp.repeat(jnp.exp(steps), extent[dim] // shards_of).reshape((-1,) + (1,) * (len(extent) - 1 - dim))
    return gain


def setup_inputs(seed: int = 0) -> dict:
    key_list = jax.random.split(jax.random.key(seed), 6)
    return {
        "launched": draw_launched(jax.random.fold_in(key_list[5], 71), 0),
        "coupling": draw_coupling(jax.random.fold_in(key_list[5], 71), 0),
        "impulse": draw_impulse(jax.random.fold_in(key_list[5], 71), 0),
        "amplifier": draw_amplifier(jax.random.fold_in(key_list[5], 71), 0),
        "nonlinear": jnp.clip(jnp.exp(math.log(0.008) - 1.3862944 * jax.random.uniform(key_list[4], (GROUPS, SPANS, STEPS), jnp.float32) ** block_scale(key_list[4], (GROUPS, SPANS, STEPS), ((0, 8),), -0.2, 0.2)), 0.002, 0.008),
    }


def split_step(signal, coupling_step, impulse_step, nonlinear_step):
    length = signal.shape[-1]
    total = length + 2 * HALF
    samples = signal[:, 0] + 1j * signal[:, 1]
    padded = jnp.pad(samples, ((0, 0), (0, 0), (HALF, HALF)))
    response = impulse_step[0] + 1j * impulse_step[1]
    kernel = jnp.concatenate([response[:1], jnp.zeros((total - 2 * HALF - 1,), response.dtype), response[:0:-1]])
    spectrum = jnp.fft.fft(padded, axis=-1) * jnp.fft.fft(kernel)[None, None, :]
    result = jnp.fft.ifft(spectrum, axis=-1)[..., :length]
    real_in = jnp.real(result)
    imag_in = jnp.imag(result)
    highest = lax.Precision.HIGHEST
    real_mat = coupling_step[0]
    imag_mat = coupling_step[1]
    real_out = jnp.einsum("cd,fdt->fct", real_mat, real_in, precision=highest) - jnp.einsum("cd,fdt->fct", imag_mat, imag_in, precision=highest)
    imag_out = jnp.einsum("cd,fdt->fct", imag_mat, real_in, precision=highest) + jnp.einsum("cd,fdt->fct", real_mat, imag_in, precision=highest)
    power = jnp.sum(real_out * real_out + imag_out * imag_out, axis=1, keepdims=True)
    phase = nonlinear_step * power
    cosine = jnp.cos(phase)
    sine = jnp.sin(phase)
    return jnp.stack([real_out * cosine - imag_out * sine, real_out * sine + imag_out * cosine], axis=1)


def reference(launched, coupling, impulse, amplifier, nonlinear):
    signal = launched
    outputs = []
    for group in range(GROUPS):
        for span_index in range(SPANS):
            for step_index in range(STEPS):
                signal = split_step(signal, coupling[group, span_index, step_index], impulse[group, span_index, step_index], nonlinear[group, span_index, step_index])
            signal = signal * amplifier[group, span_index][None, None, :, None]
        outputs.append(signal)
    return jnp.stack(outputs)
```

```python
import jax
import jax.numpy as jnp
from jax import lax
from jax.sharding import PartitionSpec as P


def band(values, width):
    padded = jnp.concatenate([values, jnp.zeros((width,), jnp.float32)])
    tiled = jnp.tile(padded, width)[: width * 2 * width]
    return tiled.reshape(width, 2 * width).T


def prepare(coupling_group, impulse_group):
    half_taps = (impulse_group.shape[-1] - 1) // 2
    width = 2 * half_taps

    def toeplitz(pair):
        real_band = band(pair[0], width)
        imag_band = band(pair[1], width)
        upper = jnp.concatenate([real_band, imag_band], axis=1)
        lower = jnp.concatenate([-imag_band, real_band], axis=1)
        return jnp.concatenate([upper, lower], axis=0)

    filters = jax.vmap(jax.vmap(toeplitz))(impulse_group)
    real_part = coupling_group[:, :, 0]
    imag_part = coupling_group[:, :, 1]
    upper = jnp.concatenate([real_part, -imag_part], axis=-1)
    lower = jnp.concatenate([imag_part, real_part], axis=-1)
    return (filters, jnp.concatenate([upper, lower], axis=-2))


def disperse(extended, matrix, half_taps):
    width = 2 * half_taps
    frames, _, channels, extent = extended.shape
    block_count = extent // width - 1
    blocks = extended.reshape(frames, 2, channels, block_count + 1, width)
    windows = jnp.concatenate([blocks[..., :-1, :], blocks[..., 1:, :]], axis=-1)
    stacked = jnp.concatenate([windows[:, 0], windows[:, 1]], axis=-1)
    product = jnp.einsum("fcbu,uv->fcbv", stacked, matrix, precision=lax.Precision.HIGHEST)
    real_part = product[..., :width].reshape(frames, channels, block_count * width)
    imag_part = product[..., width:].reshape(frames, channels, block_count * width)
    return jnp.stack([real_part, imag_part], axis=1)


def couple(signal, mixer, coefficient):
    frames, _, channels, extent = signal.shape
    flat = signal.reshape(frames, 2 * channels, extent)
    mixed = jnp.einsum("de,fel->fdl", mixer, flat, precision=lax.Precision.HIGHEST).reshape(
        frames, 2, channels, extent
    )
    power = jnp.sum(mixed * mixed, axis=(1, 2))
    phase = coefficient * power[:, None, :]
    cosine = jnp.cos(phase)
    sine = jnp.sin(phase)
    real_part = mixed[:, 0]
    imag_part = mixed[:, 1]
    return jnp.stack(
        [real_part * cosine - imag_part * sine, real_part * sine + imag_part * cosine], axis=1
    )


def neighbours(block, halo):
    count = lax.axis_size("tm")
    forward = [(i, i + 1) for i in range(count - 1)]
    backward = [(i + 1, i) for i in range(count - 1)]
    extent = block.shape[-1]
    low = lax.ppermute(lax.slice_in_dim(block, extent - halo, None, axis=3), "tm", forward)
    high = lax.ppermute(lax.slice_in_dim(block, 0, halo, axis=3), "tm", backward)
    return jnp.concatenate([low, block, high], axis=3)


def group_pass(signal, filters, mixers, amplifier_group, nonlinear_group, origin, length):
    span_count, step_count = nonlinear_group.shape
    half_taps = filters.shape[-1] // 4
    halo = span_count * step_count * half_taps
    extent = signal.shape[-1]
    signal = neighbours(signal, halo)
    offset = -halo
    for span_index in range(span_count):
        for step_index in range(step_count):
            signal = disperse(signal, filters[span_index, step_index], half_taps)
            offset = offset + half_taps
            where = origin + offset + jnp.arange(signal.shape[-1], dtype=jnp.int32)
            inside = ((where >= 0) & (where < length)).astype(jnp.float32)
            signal = signal * inside
            signal = couple(
                signal, mixers[span_index, step_index], nonlinear_group[span_index, step_index]
            )
        signal = signal * amplifier_group[span_index][None, None, :, None]
    assert signal.shape[-1] == extent
    return signal


def shards(launched, coupling, impulse, amplifier, nonlinear):
    sections = lax.axis_size("span")
    section_index = lax.axis_index("span")
    frames_count, _, _, extent = launched.shape
    per_section = frames_count // sections
    length = extent * lax.axis_size("tm")
    origin = lax.axis_index("tm") * extent

    coupling_all = lax.all_gather(coupling, "span", axis=0, tiled=True)
    impulse_all = lax.all_gather(impulse, "span", axis=0, tiled=True)
    amplifier_all = lax.all_gather(amplifier, "span", axis=0, tiled=True)
    nonlinear_all = lax.all_gather(nonlinear, "span", axis=0, tiled=True)

    signal = lax.dynamic_slice_in_dim(launched, section_index * per_section, per_section, 0)

    def advance(signal, params):
        coupling_group, impulse_group, amplifier_group, nonlinear_group = params
        filters, mixers = prepare(coupling_group, impulse_group)
        signal = group_pass(
            signal, filters, mixers, amplifier_group, nonlinear_group, origin, length
        )
        return signal, signal

    _, stacked = lax.scan(advance, signal, (coupling_all, impulse_all, amplifier_all, nonlinear_all))
    return lax.all_to_all(stacked, "span", 0, 1, tiled=True)


def solution(mesh):
    placed = (
        P(None, None, None, "tm"),
        P("span", None, None, None, None, None),
        P("span", None, None, None, None),
        P("span", None, None),
        P("span", None, None),
    )
    return jax.shard_map(
        shards,
        mesh=mesh,
        in_specs=placed,
        out_specs=P("span", None, None, None, "tm"),
        check_vma=False,
    )
```

```python
import functools

import jax
import jax.numpy as jnp
from jax import lax
from jax.sharding import PartitionSpec as P
from jax.experimental import pallas as pl
from jax.experimental.pallas import tpu as pltpu

ROWS = 128
HIGHEST = lax.Precision.HIGHEST


def band(values, width):
    padded = jnp.concatenate([values, jnp.zeros((width,), jnp.float32)])
    tiled = jnp.tile(padded, width)[: width * 2 * width]
    return tiled.reshape(width, 2 * width).T


def prepare(coupling_group, impulse_group):
    half_taps = (impulse_group.shape[-1] - 1) // 2
    width = 2 * half_taps

    def toeplitz(pair):
        real_band = band(pair[0], width)
        imag_band = band(pair[1], width)
        upper = jnp.concatenate([real_band, imag_band], axis=1)
        lower = jnp.concatenate([-imag_band, real_band], axis=1)
        return jnp.concatenate([upper, lower], axis=0)

    filters = jax.vmap(jax.vmap(toeplitz))(impulse_group)
    spans, steps = filters.shape[:2]
    filters = filters.reshape((spans * steps,) + filters.shape[2:])
    channels = coupling_group.shape[-1]
    grow = ((0, 0), (0, 0), (0, ROWS - channels), (0, ROWS - channels))
    real_part = jnp.pad(coupling_group[:, :, 0], grow)
    imag_part = jnp.pad(coupling_group[:, :, 1], grow)
    upper = jnp.concatenate([real_part, -imag_part], axis=-1)
    lower = jnp.concatenate([imag_part, real_part], axis=-1)
    mixers = jnp.concatenate([upper, lower], axis=-2)
    return (filters, mixers.reshape((spans * steps,) + mixers.shape[2:]))


def group_kernel(origin_ref, nonlinear_ref, left_ref, mid_ref, right_ref, filter_ref, mixer_ref,
                 amplifier_ref, out_ref, *, spans, steps, half_taps, length):
    width = 2 * half_taps
    halo = spans * steps * half_taps
    extent = mid_ref.shape[-1]
    origin = origin_ref[0]
    parts = []
    for part in range(2):
        parts.append(jnp.concatenate(
            [left_ref[part, :, extent - halo:], mid_ref[part], right_ref[part, :, :halo]], axis=1))
    real, imag = parts
    offset = -halo
    for span_index in range(spans):
        for step_index in range(steps):
            index = span_index * steps + step_index
            blocks = real.shape[1] // width - 1
            windows = jnp.concatenate(
                [jnp.concatenate([real[:, b * width:(b + 2) * width], imag[:, b * width:(b + 2) * width]], axis=1)
                 for b in range(blocks)], axis=0)
            product = jnp.dot(windows, filter_ref[index], precision=HIGHEST,
                              preferred_element_type=jnp.float32)
            real = jnp.concatenate([product[b * ROWS:(b + 1) * ROWS, :width] for b in range(blocks)], axis=1)
            imag = jnp.concatenate([product[b * ROWS:(b + 1) * ROWS, width:] for b in range(blocks)], axis=1)
            offset = offset + half_taps
            dispersed = jnp.concatenate([real, imag], axis=0)
            mixed = jnp.dot(mixer_ref[index], dispersed, precision=HIGHEST,
                            preferred_element_type=jnp.float32)
            where = origin + offset + lax.broadcasted_iota(jnp.int32, (1, mixed.shape[1]), 1)
            inside = (where >= 0) & (where < length)
            mixed = jnp.where(inside, mixed, 0.0)
            power = jnp.sum(mixed * mixed, axis=0, keepdims=True)
            phase = nonlinear_ref[index] * power
            cosine = jnp.cos(phase)
            sine = jnp.sin(phase)
            real_mixed = mixed[:ROWS]
            imag_mixed = mixed[ROWS:]
            real = real_mixed * cosine - imag_mixed * sine
            imag = real_mixed * sine + imag_mixed * cosine
        gain = amplifier_ref[span_index]
        real = real * gain
        imag = imag * gain
    out_ref[0] = real
    out_ref[1] = imag


def group_pass(signal, filters, mixers, amplifier_group, nonlinear_group, origin, length):
    spans, steps = nonlinear_group.shape
    half_taps = filters.shape[-1] // 4
    halo = spans * steps * half_taps
    count = lax.axis_size("tm")
    forward = [(i, i + 1) for i in range(count - 1)]
    backward = [(i + 1, i) for i in range(count - 1)]
    left = lax.ppermute(signal, "tm", forward)
    right = lax.ppermute(signal, "tm", backward)
    gain = jnp.pad(amplifier_group, ((0, 0), (0, ROWS - amplifier_group.shape[-1])))[:, :, None]
    vmem = pl.BlockSpec(memory_space=pltpu.VMEM)
    smem = pl.BlockSpec(memory_space=pltpu.SMEM)
    blocks = (signal.shape[-1] + 2 * halo) // (2 * half_taps)
    flops = 2 * spans * steps * ROWS * (blocks * 4 * half_taps * 4 * half_taps + 4 * ROWS * signal.shape[-1] * 2)
    kernel = pl.pallas_call(
        functools.partial(group_kernel, spans=spans, steps=steps, half_taps=half_taps, length=length),
        out_shape=jax.ShapeDtypeStruct(signal.shape, jnp.float32),
        in_specs=[smem, smem, vmem, vmem, vmem, vmem, vmem, vmem],
        out_specs=vmem,
        cost_estimate=pl.CostEstimate(flops=6 * flops, transcendentals=0,
                                      bytes_accessed=4 * (4 * signal.size + filters.size + mixers.size)),
    )
    return kernel(origin.reshape(1), nonlinear_group.reshape(-1), left, signal, right, filters, mixers, gain)


def shards(launched, coupling, impulse, amplifier, nonlinear):
    sections = lax.axis_size("span")
    section_index = lax.axis_index("span")
    frames_count, _, _, extent = launched.shape
    per_section = frames_count // sections
    length = extent * lax.axis_size("tm")
    origin = lax.axis_index("tm") * extent

    coupling_all = lax.all_gather(coupling, "span", axis=0, tiled=True)
    impulse_all = lax.all_gather(impulse, "span", axis=0, tiled=True)
    amplifier_all = lax.all_gather(amplifier, "span", axis=0, tiled=True)
    nonlinear_all = lax.all_gather(nonlinear, "span", axis=0, tiled=True)

    channels = launched.shape[2]
    signal = lax.dynamic_slice_in_dim(launched, section_index * per_section, per_section, 0)
    signal = jnp.pad(signal, ((0, 0), (0, 0), (0, ROWS - channels), (0, 0)))

    def advance(signal, params):
        coupling_group, impulse_group, amplifier_group, nonlinear_group = params
        filters, mixers = prepare(coupling_group, impulse_group)
        signal = jnp.stack([
            group_pass(signal[frame], filters, mixers, amplifier_group, nonlinear_group, origin, length)
            for frame in range(signal.shape[0])])
        return signal, signal

    _, stacked = lax.scan(advance, signal, (coupling_all, impulse_all, amplifier_all, nonlinear_all))
    stacked = stacked[:, :, :, :channels]
    return lax.all_to_all(stacked, "span", 0, 1, tiled=True)


def solution(mesh):
    placed = (
        P(None, None, None, "tm"),
        P("span", None, None, None, None, None),
        P("span", None, None, None, None),
        P("span", None, None),
        P("span", None, None),
    )
    return jax.shard_map(
        shards,
        mesh=mesh,
        in_specs=placed,
        out_specs=P("span", None, None, None, "tm"),
        check_vma=False,
    )
```

```python
import functools

import jax
import jax.numpy as jnp
from jax import lax
from jax.sharding import PartitionSpec as P
from jax.experimental import pallas as pl
from jax.experimental.pallas import tpu as pltpu

ROWS = 128
HIGHEST = lax.Precision.HIGHEST


def banded(row, width):
    grid = jnp.broadcast_to(row, (width, 2 * width))
    return pltpu.roll(grid, 0, 1, stride=1, stride_axis=0).T


def group_kernel(origin_ref, nonlinear_ref, left_ref, mid_ref, right_ref, taps_ref, coupling_ref,
                 amplifier_ref, out_ref, *, spans, steps, half_taps, length):
    width = 2 * half_taps
    halo = spans * steps * half_taps
    extent = mid_ref.shape[-1]
    origin = origin_ref[0]
    parts = []
    for part in range(2):
        parts.append(jnp.concatenate(
            [left_ref[part, :, extent - halo:], mid_ref[part], right_ref[part, :, :halo]], axis=1))
    real, imag = parts
    offset = -halo
    for span_index in range(spans):
        for step_index in range(steps):
            index = span_index * steps + step_index
            blocks = real.shape[1] // width - 1
            windows = jnp.concatenate(
                [jnp.concatenate([real[:, b * width:(b + 2) * width], imag[:, b * width:(b + 2) * width]], axis=1)
                 for b in range(blocks)], axis=0)
            real_band = banded(taps_ref[2 * index], width)
            imag_band = banded(taps_ref[2 * index + 1], width)
            response = jnp.concatenate([
                jnp.concatenate([real_band, imag_band], axis=1),
                jnp.concatenate([-imag_band, real_band], axis=1)], axis=0)
            product = jnp.dot(windows, response, precision=HIGHEST,
                              preferred_element_type=jnp.float32)
            real = jnp.concatenate([product[b * ROWS:(b + 1) * ROWS, :width] for b in range(blocks)], axis=1)
            imag = jnp.concatenate([product[b * ROWS:(b + 1) * ROWS, width:] for b in range(blocks)], axis=1)
            offset = offset + half_taps
            dispersed = jnp.concatenate([real, imag], axis=0)
            real_coupling = coupling_ref[2 * index]
            imag_coupling = coupling_ref[2 * index + 1]
            mixer = jnp.concatenate([
                jnp.concatenate([real_coupling, -imag_coupling], axis=1),
                jnp.concatenate([imag_coupling, real_coupling], axis=1)], axis=0)
            mixed = jnp.dot(mixer, dispersed, precision=HIGHEST,
                            preferred_element_type=jnp.float32)
            where = origin + offset + lax.broadcasted_iota(jnp.int32, (1, mixed.shape[1]), 1)
            inside = (where >= 0) & (where < length)
            mixed = jnp.where(inside, mixed, 0.0)
            power = jnp.sum(mixed * mixed, axis=0, keepdims=True)
            phase = nonlinear_ref[index] * power
            cosine = jnp.cos(phase)
            sine = jnp.sin(phase)
            real_mixed = mixed[:ROWS]
            imag_mixed = mixed[ROWS:]
            real = real_mixed * cosine - imag_mixed * sine
            imag = real_mixed * sine + imag_mixed * cosine
        gain = amplifier_ref[span_index]
        real = real * gain
        imag = imag * gain
    out_ref[0] = real
    out_ref[1] = imag


def group_pass(signal, taps, coupling, gain, nonlinear_group, origin, length, spans, steps, half_taps):
    halo = spans * steps * half_taps
    count = lax.axis_size("tm")
    forward = [(i, i + 1) for i in range(count - 1)]
    backward = [(i + 1, i) for i in range(count - 1)]
    left = lax.ppermute(signal, "tm", forward)
    right = lax.ppermute(signal, "tm", backward)
    vmem = pl.BlockSpec(memory_space=pltpu.VMEM)
    smem = pl.BlockSpec(memory_space=pltpu.SMEM)
    blocks = (signal.shape[-1] + 2 * halo) // (2 * half_taps)
    flops = 2 * spans * steps * ROWS * (blocks * 4 * half_taps * 4 * half_taps + 4 * ROWS * signal.shape[-1] * 2)
    kernel = pl.pallas_call(
        functools.partial(group_kernel, spans=spans, steps=steps, half_taps=half_taps, length=length),
        out_shape=jax.ShapeDtypeStruct(signal.shape, jnp.float32),
        in_specs=[smem, smem, vmem, vmem, vmem, vmem, vmem, vmem],
        out_specs=vmem,
        cost_estimate=pl.CostEstimate(flops=6 * flops, transcendentals=0,
                                      bytes_accessed=4 * (4 * signal.size + taps.size + coupling.size)),
    )
    return kernel(origin.reshape(1), nonlinear_group, left, signal, right, taps, coupling, gain)


def shards(launched, coupling, impulse, amplifier, nonlinear):
    sections = lax.axis_size("span")
    section_index = lax.axis_index("span")
    frames_count, _, _, extent = launched.shape
    per_section = frames_count // sections
    length = extent * lax.axis_size("tm")
    origin = lax.axis_index("tm") * extent

    pieces = (coupling, impulse, amplifier, nonlinear)
    packed = jnp.concatenate([piece.reshape(piece.shape[0], -1) for piece in pieces], axis=1)
    gathered = lax.all_gather(packed, "span", axis=0, tiled=True)
    unpacked = []
    start = 0
    for piece in pieces:
        size = piece[0].size
        unpacked.append(gathered[:, start : start + size].reshape((-1,) + piece.shape[1:]))
        start = start + size
    coupling_all, impulse_all, amplifier_all, nonlinear_all = unpacked
    groups, spans, steps, _, taps_count = impulse_all.shape
    half_taps = (taps_count - 1) // 2
    channels = launched.shape[2]
    grow = ROWS - channels
    coupling_all = jnp.pad(coupling_all, ((0, 0),) * 4 + ((0, grow), (0, grow)))
    coupling_all = coupling_all.reshape(groups, spans * steps * 2, ROWS, ROWS)
    taps_all = jnp.pad(impulse_all, ((0, 0),) * 4 + ((0, 4 * half_taps - taps_count),))
    taps_all = taps_all.reshape(groups, spans * steps * 2, 1, 4 * half_taps)
    gain_all = jnp.pad(amplifier_all, ((0, 0), (0, 0), (0, grow)))[..., None]
    nonlinear_all = nonlinear_all.reshape(groups, spans * steps)

    signal = lax.dynamic_slice_in_dim(launched, section_index * per_section, per_section, 0)
    signal = jnp.pad(signal, ((0, 0), (0, 0), (0, grow), (0, 0)))

    def advance(signal, params):
        taps, coupling_group, gain, nonlinear_group = params
        signal = jnp.stack([
            group_pass(signal[frame], taps, coupling_group, gain, nonlinear_group, origin, length,
                       spans, steps, half_taps)
            for frame in range(signal.shape[0])])
        return signal, signal

    _, stacked = lax.scan(advance, signal, (taps_all, coupling_all, gain_all, nonlinear_all))
    stacked = stacked[:, :, :, :channels]
    return lax.all_to_all(stacked, "span", 0, 1, tiled=True)


def solution(mesh):
    placed = (
        P(None, None, None, "tm"),
        P("span", None, None, None, None, None),
        P("span", None, None, None, None),
        P("span", None, None),
        P("span", None, None),
    )
    return jax.shard_map(
        shards,
        mesh=mesh,
        in_specs=placed,
        out_specs=P("span", None, None, None, "tm"),
        check_vma=False,
    )
```

```python
import functools

import jax
import jax.numpy as jnp
from jax import lax
from jax.sharding import PartitionSpec as P
from jax.experimental import pallas as pl
from jax.experimental.pallas import tpu as pltpu

ROWS = 128
HIGHEST = lax.Precision.HIGHEST


def banded(row, width):
    grid = jnp.broadcast_to(row, (width, 2 * width))
    return pltpu.roll(grid, 0, 1, stride=1, stride_axis=0).T


def group_kernel(origin_ref, nonlinear_ref, left_ref, mid_ref, right_ref, params_ref, out_ref, *,
                 spans, steps, half_taps, length):
    width = 2 * half_taps
    halo = spans * steps * half_taps
    extent = mid_ref.shape[-1]
    origin = origin_ref[0]
    matrices = 2 * spans * steps
    table = params_ref[matrices]

    def taps_row(row):
        pair = table[2 * row:2 * row + 2]
        return jnp.concatenate([pair[0:1], pair[1:2]], axis=1)

    gains = table[2 * matrices:2 * matrices + 8].T
    parts = []
    for part in range(2):
        parts.append(jnp.concatenate(
            [left_ref[part, :, extent - halo:], mid_ref[part], right_ref[part, :, :halo]], axis=1))
    real, imag = parts
    offset = -halo
    for span_index in range(spans):
        for step_index in range(steps):
            index = span_index * steps + step_index
            blocks = real.shape[1] // width - 1
            windows = jnp.concatenate(
                [jnp.concatenate([real[:, b * width:(b + 2) * width], imag[:, b * width:(b + 2) * width]], axis=1)
                 for b in range(blocks)], axis=0)
            real_band = banded(taps_row(2 * index), width)
            imag_band = banded(taps_row(2 * index + 1), width)
            response = jnp.concatenate([
                jnp.concatenate([real_band, imag_band], axis=1),
                jnp.concatenate([-imag_band, real_band], axis=1)], axis=0)
            product = jnp.dot(windows, response, precision=HIGHEST,
                              preferred_element_type=jnp.float32)
            real = jnp.concatenate([product[b * ROWS:(b + 1) * ROWS, :width] for b in range(blocks)], axis=1)
            imag = jnp.concatenate([product[b * ROWS:(b + 1) * ROWS, width:] for b in range(blocks)], axis=1)
            offset = offset + half_taps
            dispersed = jnp.concatenate([real, imag], axis=0)
            real_coupling = params_ref[2 * index]
            imag_coupling = params_ref[2 * index + 1]
            mixer = jnp.concatenate([
                jnp.concatenate([real_coupling, -imag_coupling], axis=1),
                jnp.concatenate([imag_coupling, real_coupling], axis=1)], axis=0)
            mixed = jnp.dot(mixer, dispersed, precision=HIGHEST,
                            preferred_element_type=jnp.float32)
            where = origin + offset + lax.broadcasted_iota(jnp.int32, (1, mixed.shape[1]), 1)
            inside = (where >= 0) & (where < length)
            mixed = jnp.where(inside, mixed, 0.0)
            power = jnp.sum(mixed * mixed, axis=0, keepdims=True)
            phase = nonlinear_ref[index] * power
            cosine = jnp.cos(phase)
            sine = jnp.sin(phase)
            real_mixed = mixed[:ROWS]
            imag_mixed = mixed[ROWS:]
            real = real_mixed * cosine - imag_mixed * sine
            imag = real_mixed * sine + imag_mixed * cosine
        gain = gains[:, span_index:span_index + 1]
        real = real * gain
        imag = imag * gain
    out_ref[0] = real
    out_ref[1] = imag


def group_pass(signal, params, origin, length, spans, steps, half_taps):
    halo = spans * steps * half_taps
    count = lax.axis_size("tm")
    forward = [(i, i + 1) for i in range(count - 1)]
    backward = [(i + 1, i) for i in range(count - 1)]
    left = lax.ppermute(signal, "tm", forward)
    right = lax.ppermute(signal, "tm", backward)
    matrices = 2 * spans * steps
    nonlinear_group = params[matrices, 2 * matrices + 8, : spans * steps]
    vmem = pl.BlockSpec(memory_space=pltpu.VMEM)
    smem = pl.BlockSpec(memory_space=pltpu.SMEM)
    blocks = (signal.shape[-1] + 2 * halo) // (2 * half_taps)
    flops = 2 * spans * steps * ROWS * (blocks * 4 * half_taps * 4 * half_taps + 4 * ROWS * signal.shape[-1] * 2)
    kernel = pl.pallas_call(
        functools.partial(group_kernel, spans=spans, steps=steps, half_taps=half_taps, length=length),
        out_shape=jax.ShapeDtypeStruct(signal.shape, jnp.float32),
        in_specs=[smem, smem, vmem, vmem, vmem, vmem],
        out_specs=vmem,
        cost_estimate=pl.CostEstimate(flops=6 * flops, transcendentals=0,
                                      bytes_accessed=4 * (4 * signal.size + params.size)),
    )
    return kernel(origin.reshape(1), nonlinear_group, left, signal, right, params)


def shards(launched, coupling, impulse, amplifier, nonlinear):
    sections = lax.axis_size("span")
    section_index = lax.axis_index("span")
    frames_count, _, _, extent = launched.shape
    per_section = frames_count // sections
    length = extent * lax.axis_size("tm")
    origin = lax.axis_index("tm") * extent

    local_groups, spans, steps, _, taps_count = impulse.shape
    groups = local_groups * sections
    half_taps = (taps_count - 1) // 2
    channels = launched.shape[2]
    grow = ROWS - channels
    matrices = 2 * spans * steps
    assert 4 * matrices + 16 <= ROWS and 4 * half_taps == 2 * ROWS and spans <= 8
    taps_rows = jnp.pad(impulse, ((0, 0),) * 4 + ((0, 4 * half_taps - taps_count),)).reshape(
        local_groups, 2 * matrices, ROWS)
    gain_rows = jnp.pad(amplifier, ((0, 0), (0, 8 - spans), (0, grow)))
    nonlinear_rows = jnp.pad(nonlinear.reshape(local_groups, 1, spans * steps),
                             ((0, 0), (0, 0), (0, ROWS - spans * steps)))
    table = jnp.concatenate([taps_rows, gain_rows, nonlinear_rows], axis=1)
    table = jnp.pad(table, ((0, 0), (0, ROWS - table.shape[1]), (0, 0)))
    local = jnp.concatenate([
        jnp.pad(coupling, ((0, 0),) * 4 + ((0, grow), (0, grow))).reshape(
            local_groups, matrices, ROWS, ROWS),
        table[:, None]], axis=1)

    def fetched(group):
        owner = group // local_groups
        chosen = lax.dynamic_index_in_dim(local, group % local_groups, 0, keepdims=False)
        return lax.psum(jnp.where(section_index == owner, chosen, 0.0), "span")

    signal = lax.dynamic_slice_in_dim(launched, section_index * per_section, per_section, 0)
    signal = jnp.pad(signal, ((0, 0), (0, 0), (0, grow), (0, 0)))

    def advance(carry, group):
        signal, params = carry
        upcoming = fetched(jnp.minimum(group + 1, groups - 1))
        signal = jnp.stack([
            group_pass(signal[frame], params, origin, length, spans, steps, half_taps)
            for frame in range(signal.shape[0])])
        return (signal, upcoming), signal

    start = (signal, fetched(jnp.int32(0)))
    _, stacked = lax.scan(advance, start, jnp.arange(groups, dtype=jnp.int32))
    stacked = stacked[:, :, :, :channels]
    return lax.all_to_all(stacked, "span", 0, 1, tiled=True)


def solution(mesh):
    placed = (
        P(None, None, None, "tm"),
        P("span", None, None, None, None, None),
        P("span", None, None, None, None),
        P("span", None, None),
        P("span", None, None),
    )
    return jax.shard_map(
        shards,
        mesh=mesh,
        in_specs=placed,
        out_specs=P("span", None, None, None, "tm"),
        check_vma=False,
    )
```

```python
import functools

import jax
import jax.numpy as jnp
from jax import lax
from jax.sharding import PartitionSpec as P
from jax.experimental import pallas as pl
from jax.experimental.pallas import tpu as pltpu

ROWS = 128
HIGHEST = lax.Precision.HIGHEST


def banded(row, width):
    grid = jnp.broadcast_to(row, (width, 2 * width))
    return pltpu.roll(grid, 0, 1, stride=1, stride_axis=0).T


def group_kernel(scalar_ref, nonlinear_ref, left_ref, mid_ref, right_ref, taps_ref, coupling_ref,
                 amplifier_ref, out_ref, *, spans, steps, half_taps, length):
    width = 2 * half_taps
    halo = spans * steps * half_taps
    extent = mid_ref.shape[-1]
    group = scalar_ref[0]
    origin = scalar_ref[1]
    parts = []
    for part in range(2):
        parts.append(jnp.concatenate(
            [left_ref[part, :, extent - halo:], mid_ref[part], right_ref[part, :, :halo]], axis=1))
    real, imag = parts
    offset = -halo
    for span_index in range(spans):
        for step_index in range(steps):
            index = span_index * steps + step_index
            blocks = real.shape[1] // width - 1
            windows = jnp.concatenate(
                [jnp.concatenate([real[:, b * width:(b + 2) * width], imag[:, b * width:(b + 2) * width]], axis=1)
                 for b in range(blocks)], axis=0)
            real_band = banded(taps_ref[0, 2 * index], width)
            imag_band = banded(taps_ref[0, 2 * index + 1], width)
            response = jnp.concatenate([
                jnp.concatenate([real_band, imag_band], axis=1),
                jnp.concatenate([-imag_band, real_band], axis=1)], axis=0)
            product = jnp.dot(windows, response, precision=HIGHEST,
                              preferred_element_type=jnp.float32)
            real = jnp.concatenate([product[b * ROWS:(b + 1) * ROWS, :width] for b in range(blocks)], axis=1)
            imag = jnp.concatenate([product[b * ROWS:(b + 1) * ROWS, width:] for b in range(blocks)], axis=1)
            offset = offset + half_taps
            dispersed = jnp.concatenate([real, imag], axis=0)
            real_coupling = coupling_ref[0, 2 * index]
            imag_coupling = coupling_ref[0, 2 * index + 1]
            mixer = jnp.concatenate([
                jnp.concatenate([real_coupling, -imag_coupling], axis=1),
                jnp.concatenate([imag_coupling, real_coupling], axis=1)], axis=0)
            mixed = jnp.dot(mixer, dispersed, precision=HIGHEST,
                            preferred_element_type=jnp.float32)
            where = origin + offset + lax.broadcasted_iota(jnp.int32, (1, mixed.shape[1]), 1)
            inside = (where >= 0) & (where < length)
            mixed = jnp.where(inside, mixed, 0.0)
            power = jnp.sum(mixed * mixed, axis=0, keepdims=True)
            phase = nonlinear_ref[group, index] * power
            cosine = jnp.cos(phase)
            sine = jnp.sin(phase)
            real_mixed = mixed[:ROWS]
            imag_mixed = mixed[ROWS:]
            real = real_mixed * cosine - imag_mixed * sine
            imag = real_mixed * sine + imag_mixed * cosine
        gain = amplifier_ref[0, span_index]
        real = real * gain
        imag = imag * gain
    out_ref[0] = real
    out_ref[1] = imag


def group_pass(signal, group, taps, coupling, gain, nonlinear, origin, length, spans, steps, half_taps):
    halo = spans * steps * half_taps
    count = lax.axis_size("tm")
    forward = [(i, i + 1) for i in range(count - 1)]
    backward = [(i + 1, i) for i in range(count - 1)]
    left = lax.ppermute(signal, "tm", forward)
    right = lax.ppermute(signal, "tm", backward)
    smem = pl.BlockSpec(memory_space=pltpu.SMEM)

    def whole(shape):
        return pl.BlockSpec(shape, lambda i, scalars: (0,) * len(shape))

    def chosen(array):
        shape = (1,) + array.shape[1:]
        return pl.BlockSpec(shape, lambda i, scalars: (scalars[0],) + (0,) * (len(shape) - 1))

    blocks = (signal.shape[-1] + 2 * halo) // (2 * half_taps)
    flops = 2 * spans * steps * ROWS * (blocks * 4 * half_taps * 4 * half_taps + 4 * ROWS * signal.shape[-1] * 2)
    grid_spec = pltpu.PrefetchScalarGridSpec(
        num_scalar_prefetch=1,
        grid=(1,),
        in_specs=[smem, whole(signal.shape), whole(signal.shape), whole(signal.shape),
                  chosen(taps), chosen(coupling), chosen(gain)],
        out_specs=whole(signal.shape),
    )
    kernel = pl.pallas_call(
        functools.partial(group_kernel, spans=spans, steps=steps, half_taps=half_taps, length=length),
        out_shape=jax.ShapeDtypeStruct(signal.shape, jnp.float32),
        grid_spec=grid_spec,
        cost_estimate=pl.CostEstimate(flops=6 * flops, transcendentals=0,
                                      bytes_accessed=4 * (4 * signal.size + taps[0].size + coupling[0].size)),
    )
    scalars = jnp.stack([group, origin]).astype(jnp.int32)
    return kernel(scalars, nonlinear, left, signal, right, taps, coupling, gain)


def shards(launched, coupling, impulse, amplifier, nonlinear):
    sections = lax.axis_size("span")
    section_index = lax.axis_index("span")
    frames_count, _, _, extent = launched.shape
    per_section = frames_count // sections
    length = extent * lax.axis_size("tm")
    origin = lax.axis_index("tm") * extent

    pieces = (coupling, impulse, amplifier, nonlinear)
    packed = jnp.concatenate([piece.reshape(piece.shape[0], -1) for piece in pieces], axis=1)
    gathered = lax.all_gather(packed, "span", axis=0, tiled=True)
    unpacked = []
    start = 0
    for piece in pieces:
        size = piece[0].size
        unpacked.append(gathered[:, start : start + size].reshape((-1,) + piece.shape[1:]))
        start = start + size
    coupling_all, impulse_all, amplifier_all, nonlinear_all = unpacked
    groups, spans, steps, _, taps_count = impulse_all.shape
    half_taps = (taps_count - 1) // 2
    channels = launched.shape[2]
    grow = ROWS - channels
    coupling_all = jnp.pad(coupling_all, ((0, 0),) * 4 + ((0, grow), (0, grow)))
    coupling_all = coupling_all.reshape(groups, spans * steps * 2, ROWS, ROWS)
    taps_all = jnp.pad(impulse_all, ((0, 0),) * 4 + ((0, 4 * half_taps - taps_count),))
    taps_all = taps_all.reshape(groups, spans * steps * 2, 1, 4 * half_taps)
    gain_all = jnp.pad(amplifier_all, ((0, 0), (0, 0), (0, grow)))[..., None]
    nonlinear_all = nonlinear_all.reshape(groups, spans * steps)

    signal = lax.dynamic_slice_in_dim(launched, section_index * per_section, per_section, 0)
    signal = jnp.pad(signal, ((0, 0), (0, 0), (0, grow), (0, 0)))

    def advance(signal, group):
        signal = jnp.stack([
            group_pass(signal[frame], group, taps_all, coupling_all, gain_all, nonlinear_all, origin,
                       length, spans, steps, half_taps)
            for frame in range(signal.shape[0])])
        return signal, signal

    _, stacked = lax.scan(advance, signal, jnp.arange(groups, dtype=jnp.int32))
    stacked = stacked[:, :, :, :channels]
    return lax.all_to_all(stacked, "span", 0, 1, tiled=True)


def solution(mesh):
    placed = (
        P(None, None, None, "tm"),
        P("span", None, None, None, None, None),
        P("span", None, None, None, None),
        P("span", None, None),
        P("span", None, None),
    )
    return jax.shard_map(
        shards,
        mesh=mesh,
        in_specs=placed,
        out_specs=P("span", None, None, None, "tm"),
        check_vma=False,
    )
```

```python
import functools

import jax
import jax.numpy as jnp
from jax import lax
from jax.sharding import PartitionSpec as P
from jax.experimental import pallas as pl
from jax.experimental.pallas import tpu as pltpu

ROWS = 128
HIGHEST = lax.Precision.HIGHEST


def banded(row, width):
    grid = jnp.broadcast_to(row, (width, 2 * width))
    return pltpu.roll(grid, 0, 1, stride=1, stride_axis=0).T


def group_kernel(scalar_ref, nonlinear_ref, left_ref, mid_ref, right_ref, taps_ref, coupling_ref,
                 amplifier_ref, out_ref, *, spans, steps, half_taps, length):
    width = 2 * half_taps
    halo = spans * steps * half_taps
    extent = mid_ref.shape[-1]
    group = scalar_ref[0]
    origin = scalar_ref[1]
    parts = []
    for part in range(2):
        parts.append(jnp.concatenate(
            [left_ref[part, :, extent - halo:], mid_ref[part], right_ref[part, :, :halo]], axis=1))
    real, imag = parts
    offset = -halo
    for span_index in range(spans):
        for step_index in range(steps):
            index = span_index * steps + step_index
            blocks = real.shape[1] // width - 1
            windows = jnp.concatenate(
                [jnp.concatenate([real[:, b * width:(b + 2) * width], imag[:, b * width:(b + 2) * width]], axis=1)
                 for b in range(blocks)], axis=0)
            real_band = banded(taps_ref[0, 2 * index], width)
            imag_band = banded(taps_ref[0, 2 * index + 1], width)
            response = jnp.concatenate([
                jnp.concatenate([real_band, imag_band], axis=1),
                jnp.concatenate([-imag_band, real_band], axis=1)], axis=0)
            product = jnp.dot(windows, response, precision=HIGHEST,
                              preferred_element_type=jnp.float32)
            real = jnp.concatenate([product[b * ROWS:(b + 1) * ROWS, :width] for b in range(blocks)], axis=1)
            imag = jnp.concatenate([product[b * ROWS:(b + 1) * ROWS, width:] for b in range(blocks)], axis=1)
            offset = offset + half_taps
            dispersed = jnp.concatenate([real, imag], axis=0)
            real_coupling = coupling_ref[0, 2 * index]
            imag_coupling = coupling_ref[0, 2 * index + 1]
            mixer = jnp.concatenate([
                jnp.concatenate([real_coupling, -imag_coupling], axis=1),
                jnp.concatenate([imag_coupling, real_coupling], axis=1)], axis=0)
            mixed = jnp.dot(mixer, dispersed, precision=HIGHEST,
                            preferred_element_type=jnp.float32)
            where = origin + offset + lax.broadcasted_iota(jnp.int32, (1, mixed.shape[1]), 1)
            inside = (where >= 0) & (where < length)
            mixed = jnp.where(inside, mixed, 0.0)
            power = jnp.sum(mixed * mixed, axis=0, keepdims=True)
            phase = nonlinear_ref[group, index] * power
            cosine = jnp.cos(phase)
            sine = jnp.sin(phase)
            real_mixed = mixed[:ROWS]
            imag_mixed = mixed[ROWS:]
            real = real_mixed * cosine - imag_mixed * sine
            imag = real_mixed * sine + imag_mixed * cosine
        gain = amplifier_ref[0, span_index]
        real = real * gain
        imag = imag * gain
    out_ref[0] = real
    out_ref[1] = imag


def exchanged(signal):
    count = lax.axis_size("tm")
    forward = [(i, i + 1) for i in range(count - 1)]
    backward = [(i + 1, i) for i in range(count - 1)]
    return lax.ppermute(signal, "tm", forward), lax.ppermute(signal, "tm", backward)


def group_pass(signal, left, right, group, taps, coupling, gain, nonlinear, origin, length, spans,
               steps, half_taps):
    halo = spans * steps * half_taps
    smem = pl.BlockSpec(memory_space=pltpu.SMEM)

    def whole(shape):
        return pl.BlockSpec(shape, lambda i, scalars: (0,) * len(shape))

    def chosen(array):
        shape = (1,) + array.shape[1:]
        return pl.BlockSpec(shape, lambda i, scalars: (scalars[0],) + (0,) * (len(shape) - 1))

    blocks = (signal.shape[-1] + 2 * halo) // (2 * half_taps)
    flops = 2 * spans * steps * ROWS * (blocks * 4 * half_taps * 4 * half_taps + 4 * ROWS * signal.shape[-1] * 2)
    grid_spec = pltpu.PrefetchScalarGridSpec(
        num_scalar_prefetch=1,
        grid=(1,),
        in_specs=[smem, whole(signal.shape), whole(signal.shape), whole(signal.shape),
                  chosen(taps), chosen(coupling), chosen(gain)],
        out_specs=whole(signal.shape),
    )
    kernel = pl.pallas_call(
        functools.partial(group_kernel, spans=spans, steps=steps, half_taps=half_taps, length=length),
        out_shape=jax.ShapeDtypeStruct(signal.shape, jnp.float32),
        grid_spec=grid_spec,
        cost_estimate=pl.CostEstimate(flops=6 * flops, transcendentals=0,
                                      bytes_accessed=4 * (4 * signal.size + taps[0].size + coupling[0].size)),
    )
    scalars = jnp.stack([group, origin]).astype(jnp.int32)
    return kernel(scalars, nonlinear, left, signal, right, taps, coupling, gain)


def shards(launched, coupling, impulse, amplifier, nonlinear):
    sections = lax.axis_size("span")
    section_index = lax.axis_index("span")
    frames_count, _, _, extent = launched.shape
    per_section = frames_count // sections
    length = extent * lax.axis_size("tm")
    origin = lax.axis_index("tm") * extent

    pieces = (coupling, impulse, amplifier, nonlinear)
    packed = jnp.concatenate([piece.reshape(piece.shape[0], -1) for piece in pieces], axis=1)
    gathered = lax.all_gather(packed, "span", axis=0, tiled=True)
    unpacked = []
    start = 0
    for piece in pieces:
        size = piece[0].size
        unpacked.append(gathered[:, start : start + size].reshape((-1,) + piece.shape[1:]))
        start = start + size
    coupling_all, impulse_all, amplifier_all, nonlinear_all = unpacked
    groups, spans, steps, _, taps_count = impulse_all.shape
    half_taps = (taps_count - 1) // 2
    channels = launched.shape[2]
    grow = ROWS - channels
    coupling_all = jnp.pad(coupling_all, ((0, 0),) * 4 + ((0, grow), (0, grow)))
    coupling_all = coupling_all.reshape(groups, spans * steps * 2, ROWS, ROWS)
    taps_all = jnp.pad(impulse_all, ((0, 0),) * 4 + ((0, 4 * half_taps - taps_count),))
    taps_all = taps_all.reshape(groups, spans * steps * 2, 1, 4 * half_taps)
    gain_all = jnp.pad(amplifier_all, ((0, 0), (0, 0), (0, grow)))[..., None]
    nonlinear_all = nonlinear_all.reshape(groups, spans * steps)

    signal = lax.dynamic_slice_in_dim(launched, section_index * per_section, per_section, 0)
    signal = jnp.pad(signal, ((0, 0), (0, 0), (0, grow), (0, 0)))

    def passed(signal, left, right, group):
        return group_pass(signal, left, right, group, taps_all, coupling_all, gain_all, nonlinear_all,
                          origin, length, spans, steps, half_taps)

    signal = signal[0]
    assert per_section == 1
    left, right = exchanged(signal)

    def advance(carry, group):
        signal, left, right = carry
        signal = passed(signal, left, right, group)
        left, right = exchanged(signal)
        return (signal, left, right), signal

    (signal, left, right), stacked = lax.scan(
        advance, (signal, left, right), jnp.arange(groups - 1, dtype=jnp.int32))
    last = passed(signal, left, right, jnp.int32(groups - 1))
    stacked = jnp.concatenate([stacked, last[None]], axis=0)[:, None]
    stacked = stacked[:, :, :, :channels]
    return lax.all_to_all(stacked, "span", 0, 1, tiled=True)


def solution(mesh):
    placed = (
        P(None, None, None, "tm"),
        P("span", None, None, None, None, None),
        P("span", None, None, None, None),
        P("span", None, None),
        P("span", None, None),
    )
    return jax.shard_map(
        shards,
        mesh=mesh,
        in_specs=placed,
        out_specs=P("span", None, None, None, "tm"),
        check_vma=False,
    )
```

```python
import functools

import jax
import jax.numpy as jnp
from jax import lax
from jax.sharding import PartitionSpec as P
from jax.experimental import pallas as pl
from jax.experimental.pallas import tpu as pltpu

ROWS = 128
HIGHEST = lax.Precision.HIGHEST


def banded(row, width):
    grid = jnp.broadcast_to(row, (width, 2 * width))
    return pltpu.roll(grid, 0, 1, stride=1, stride_axis=0).T


def group_kernel(scalar_ref, nonlinear_ref, left_ref, mid_ref, right_ref, taps_ref, coupling_ref,
                 amplifier_ref, out_ref, *, spans, steps, half_taps, length):
    width = 2 * half_taps
    halo = spans * steps * half_taps
    extent = mid_ref.shape[-1]
    group = scalar_ref[0]
    origin = scalar_ref[1]
    parts = []
    for part in range(2):
        parts.append(jnp.concatenate(
            [left_ref[part, :, extent - halo:], mid_ref[part], right_ref[part, :, :halo]], axis=1))
    real, imag = parts
    offset = -halo
    for span_index in range(spans):
        for step_index in range(steps):
            index = span_index * steps + step_index
            blocks = real.shape[1] // width - 1
            windows = jnp.concatenate(
                [jnp.concatenate([real[:, b * width:(b + 2) * width], imag[:, b * width:(b + 2) * width]], axis=1)
                 for b in range(blocks)], axis=0)
            real_band = banded(taps_ref[0, 2 * index], width)
            imag_band = banded(taps_ref[0, 2 * index + 1], width)
            response = jnp.concatenate([
                jnp.concatenate([real_band, imag_band], axis=1),
                jnp.concatenate([-imag_band, real_band], axis=1)], axis=0)
            product = jnp.dot(windows, response, precision=HIGHEST,
                              preferred_element_type=jnp.float32)
            real = jnp.concatenate([product[b * ROWS:(b + 1) * ROWS, :width] for b in range(blocks)], axis=1)
            imag = jnp.concatenate([product[b * ROWS:(b + 1) * ROWS, width:] for b in range(blocks)], axis=1)
            offset = offset + half_taps
            dispersed = jnp.concatenate([real, imag], axis=0)
            real_coupling = coupling_ref[0, 2 * index]
            imag_coupling = coupling_ref[0, 2 * index + 1]
            mixer = jnp.concatenate([
                jnp.concatenate([real_coupling, -imag_coupling], axis=1),
                jnp.concatenate([imag_coupling, real_coupling], axis=1)], axis=0)
            mixed = jnp.dot(mixer, dispersed, precision=HIGHEST,
                            preferred_element_type=jnp.float32)
            where = origin + offset + lax.broadcasted_iota(jnp.int32, (1, mixed.shape[1]), 1)
            inside = (where >= 0) & (where < length)
            mixed = jnp.where(inside, mixed, 0.0)
            power = jnp.sum(mixed * mixed, axis=0, keepdims=True)
            phase = nonlinear_ref[group, index] * power
            cosine = jnp.cos(phase)
            sine = jnp.sin(phase)
            real_mixed = mixed[:ROWS]
            imag_mixed = mixed[ROWS:]
            real = real_mixed * cosine - imag_mixed * sine
            imag = real_mixed * sine + imag_mixed * cosine
        gain = amplifier_ref[0, span_index]
        real = real * gain
        imag = imag * gain
    out_ref[0] = real
    out_ref[1] = imag


def group_pass(signal, group, taps, coupling, gain, nonlinear, origin, length, spans, steps, half_taps):
    halo = spans * steps * half_taps
    count = lax.axis_size("tm")
    forward = [(i, i + 1) for i in range(count - 1)]
    backward = [(i + 1, i) for i in range(count - 1)]
    left = lax.ppermute(signal, "tm", forward)
    right = lax.ppermute(signal, "tm", backward)
    smem = pl.BlockSpec(memory_space=pltpu.SMEM)

    def whole(shape):
        return pl.BlockSpec(shape, lambda i, scalars: (0,) * len(shape))

    def chosen(array):
        shape = (1,) + array.shape[1:]
        return pl.BlockSpec(shape, lambda i, scalars: (scalars[0],) + (0,) * (len(shape) - 1))

    blocks = (signal.shape[-1] + 2 * halo) // (2 * half_taps)
    flops = 2 * spans * steps * ROWS * (blocks * 4 * half_taps * 4 * half_taps + 4 * ROWS * signal.shape[-1] * 2)
    grid_spec = pltpu.PrefetchScalarGridSpec(
        num_scalar_prefetch=1,
        grid=(1,),
        in_specs=[smem, whole(signal.shape), whole(signal.shape), whole(signal.shape),
                  chosen(taps), chosen(coupling), chosen(gain)],
        out_specs=whole(signal.shape),
    )
    kernel = pl.pallas_call(
        functools.partial(group_kernel, spans=spans, steps=steps, half_taps=half_taps, length=length),
        out_shape=jax.ShapeDtypeStruct(signal.shape, jnp.float32),
        grid_spec=grid_spec,
        cost_estimate=pl.CostEstimate(flops=6 * flops, transcendentals=0,
                                      bytes_accessed=4 * (4 * signal.size + taps[0].size + coupling[0].size)),
    )
    scalars = jnp.stack([group, origin]).astype(jnp.int32)
    return kernel(scalars, nonlinear, left, signal, right, taps, coupling, gain)


def shards(launched, coupling, impulse, amplifier, nonlinear):
    sections = lax.axis_size("span")
    section_index = lax.axis_index("span")
    frames_count, _, _, extent = launched.shape
    per_section = frames_count // sections
    length = extent * lax.axis_size("tm")
    origin = lax.axis_index("tm") * extent

    pieces = (coupling, impulse, amplifier, nonlinear)
    packed = jnp.concatenate([piece.reshape(piece.shape[0], -1) for piece in pieces], axis=1)
    parts = lax.axis_size("tm")
    size = packed.shape[1]
    chunk = -(-size // (parts * 128)) * 128
    packed = jnp.pad(packed, ((0, 0), (0, chunk * parts - size))).reshape(1, parts, chunk)
    mine = lax.dynamic_index_in_dim(packed, lax.axis_index("tm"), 1, keepdims=False)
    across = lax.all_gather(mine, "span", axis=0, tiled=True)
    gathered = lax.all_gather(across, "tm", axis=1, tiled=True)[:, :size]
    unpacked = []
    start = 0
    for piece in pieces:
        size = piece[0].size
        unpacked.append(gathered[:, start : start + size].reshape((-1,) + piece.shape[1:]))
        start = start + size
    coupling_all, impulse_all, amplifier_all, nonlinear_all = unpacked
    groups, spans, steps, _, taps_count = impulse_all.shape
    half_taps = (taps_count - 1) // 2
    channels = launched.shape[2]
    grow = ROWS - channels
    coupling_all = jnp.pad(coupling_all, ((0, 0),) * 4 + ((0, grow), (0, grow)))
    coupling_all = coupling_all.reshape(groups, spans * steps * 2, ROWS, ROWS)
    taps_all = jnp.pad(impulse_all, ((0, 0),) * 4 + ((0, 4 * half_taps - taps_count),))
    taps_all = taps_all.reshape(groups, spans * steps * 2, 1, 4 * half_taps)
    gain_all = jnp.pad(amplifier_all, ((0, 0), (0, 0), (0, grow)))[..., None]
    nonlinear_all = nonlinear_all.reshape(groups, spans * steps)

    signal = lax.dynamic_slice_in_dim(launched, section_index * per_section, per_section, 0)
    signal = jnp.pad(signal, ((0, 0), (0, 0), (0, grow), (0, 0)))

    def advance(signal, group):
        signal = jnp.stack([
            group_pass(signal[frame], group, taps_all, coupling_all, gain_all, nonlinear_all, origin,
                       length, spans, steps, half_taps)
            for frame in range(signal.shape[0])])
        return signal, signal

    _, stacked = lax.scan(advance, signal, jnp.arange(groups, dtype=jnp.int32))
    stacked = stacked[:, :, :, :channels]
    return lax.all_to_all(stacked, "span", 0, 1, tiled=True)


def solution(mesh):
    placed = (
        P(None, None, None, "tm"),
        P("span", None, None, None, None, None),
        P("span", None, None, None, None),
        P("span", None, None),
        P("span", None, None),
    )
    return jax.shard_map(
        shards,
        mesh=mesh,
        in_specs=placed,
        out_specs=P("span", None, None, None, "tm"),
        check_vma=False,
    )
```
